128 devices in a mesh: shard: 8 (over x, core), tensor: 16 (over z, y).
Axes of the slice: x: 4, y: 4, z: 4, core: 2. Of those that a mesh axis runs over, the one named last changes fastest.
Arguments:
- grad_square: bfloat16 [8, 768, 768], P(None, 'shard'), may hold values from -64 to 64
- grad_wide: bfloat16 [8, 2048, 768], P(None, 'shard'), may hold values from -64 to 64
- moment_square: float32 [8, 589824], P(None, ('shard', 'tensor')), may hold values from -6 to 6
- moment_wide: float32 [8, 1572864], P(None, ('shard', 'tensor')), may hold values from -6 to 6
Outputs:
- update_square: float32 [8, 768, 768], P(None, 'shard')
- update_wide: float32 [8, 2048, 768], P(None, 'shard')
- new_moment_square: float32 [8, 589824], P(None, ('shard', 'tensor'))
- new_moment_wide: float32 [8, 1572864], P(None, ('shard', 'tensor'))
The draws below stay inside these ranges and needn't reach their ends.
All inputs are finite; a program needn't handle non-finite values.
Results may differ from the reference program's by a relative error of at most 0.0003.
Values sent between devices are 32-bit elements; how exact they have to be, the bound alone decides.
No kernel may reach another device: no remote copies, remote signals or barrier semaphores. Data moves between devices by JAX's collectives and lax.ppermute only.
A program may use at most 128 MiB of HBM per device.

```python
import math
import jax
import jax.numpy as jnp
from jax import lax

D = 768
FF = 2048
ITERS = 3
NSQ = 8
NW = 8


def scaled_draw(key, matrix_count, row_count, columns):
    key_noise, key_row, key_col = jax.random.split(key, 3)
    position = jnp.arange(row_count, dtype=jnp.float32) / float(row_count - 1)
    rising = jnp.exp((position - 1.0) * math.log(3.0))[None, :, None]
    noise = jnp.clip(jax.random.normal(key_noise, (matrix_count, row_count, columns), jnp.float32), -6.0, 6.0)
    half_range = 0.5 * math.log(10.0)
    row_scale = jnp.exp(jax.random.uniform(key_row, (matrix_count, row_count, 1), jnp.float32, -half_range, half_range))
    col_scale = jnp.exp(jax.random.uniform(key_col, (matrix_count, 1, columns), jnp.float32, -half_range, half_range))
    return noise * row_scale * col_scale * rising


def draw_grad_square(key, part):
    return scaled_draw(jax.random.fold_in(key, 11), NSQ, D, D).astype(jnp.bfloat16)


def draw_grad_wide(key, part):
    return scaled_draw(jax.random.fold_in(key, 23), NW, FF, D).astype(jnp.bfloat16)


def block_scale(stream_key, extent, cuts, least, largest):
    level = 1.0
    for dim, blocks in cuts:
        steps = jax.random.uniform(jax.random.fold_in(jax.random.fold_in(stream_key, 6), dim), (blocks,), jnp.float32, least / len(cuts), largest / len(cuts))
        level = level * jnp.repeat(jnp.exp(steps), extent[dim] // blocks).reshape((-1,) + (1,) * (len(extent) - 1 - dim))
    return level


def bell_draw(stream_key, shape, deviation, bound, cuts=(), kind=jnp.bfloat16):
    level = block_scale(stream_key, shape, cuts, -0.22, 0.18) if cuts else 1.0
    array = jax.random.normal(stream_key, shape, jnp.float32) * deviation * level
    return jnp.minimum(jnp.maximum(array, -bound), bound).astype(kind)


def setup_inputs(seed: int = 0) -> dict:
    keys = jax.random.split(jax.random.key(seed), 5)
    return {
        "grad_square": draw_grad_square(jax.random.fold_in(keys[4], 71), 0),
        "grad_wide": draw_grad_wide(jax.random.fold_in(keys[4], 71), 0),
        "moment_square": bell_draw(keys[2], (NSQ, D * D), 1.0, 6.0, ((1, 128),), jnp.float32),
        "moment_wide": bell_draw(keys[3], (NW, FF * D), 1.0, 6.0, ((1, 128),), jnp.float32),
    }


coef_a = 3.4445
coef_b = -4.775
coef_c = 2.0315
momentum_decay = 0.95
epsilon = 1e-07

def orthogonalize(look):
    row_total = look.shape[0]
    current = look / (jnp.sqrt(jnp.sum(look * look)) + epsilon)
    for iteration in range(ITERS):
        gram = jnp.dot(current.T, current, precision=lax.Precision.HIGHEST, preferred_element_type=jnp.float32)
        square_gram = jnp.dot(gram, gram, precision=lax.Precision.HIGHEST, preferred_element_type=jnp.float32)
        mixer = coef_b * gram + coef_c * square_gram
        product = jnp.dot(current, mixer, precision=lax.Precision.HIGHEST, preferred_element_type=jnp.float32)
        current = coef_a * current + product
    return math.sqrt(row_total) * current

def advance(grad, moment):
    grad_float = grad.astype(jnp.float32)
    new_moment = momentum_decay * moment.reshape(grad.shape) + grad_float
    look = grad_float + momentum_decay * new_moment
    update = lax.map(orthogonalize, look)
    return (update, new_moment.reshape(moment.shape))

def reference(grad_square, grad_wide, moment_square, moment_wide):
    update_square, new_moment_square = advance(grad_square, moment_square)
    update_wide, new_moment_wide = advance(grad_wide, moment_wide)
    return (update_square, update_wide, new_moment_square, new_moment_wide)
```

```python
import math

import jax
import jax.numpy as jnp
from jax import lax
from jax.sharding import PartitionSpec as P

D = 768
FF = 2048
ITERS = 3


coef_a = 3.4445
coef_b = -4.775
coef_c = 2.0315
momentum_decay = 0.95
epsilon = 1e-07

HIGHEST = lax.Precision.HIGHEST


def dot(x, y):
    return jnp.dot(x, y, precision=HIGHEST, preferred_element_type=jnp.float32)


def gram_of(rows):
    return lax.dot_general(
        rows,
        rows,
        (((0,), (0,)), ((), ())),
        precision=HIGHEST,
        preferred_element_type=jnp.float32,
    )


def own_rows(grad, member, tensor_count):
    row_piece = grad.shape[1] // tensor_count
    return lax.dynamic_slice_in_dim(grad, member * row_piece, row_piece, 1)


def shards(grad_square, grad_wide, moment_square, moment_wide):
    tensor_count = lax.axis_size("tensor")
    member = lax.axis_index("tensor")
    count_square, count_wide = grad_square.shape[0], grad_wide.shape[0]
    assert count_square == count_wide and 2 * count_square == tensor_count
    flat_square = own_rows(grad_square, member, tensor_count).astype(jnp.float32)
    flat_wide = own_rows(grad_wide, member, tensor_count).astype(jnp.float32)
    new_square = momentum_decay * moment_square.reshape(flat_square.shape) + flat_square
    new_wide = momentum_decay * moment_wide.reshape(flat_wide.shape) + flat_wide
    look_square = flat_square + momentum_decay * new_square
    look_wide = flat_wide + momentum_decay * new_wide

    piece = look_wide.shape[1]
    pad = piece - look_square.shape[1]
    padded_square = jnp.pad(look_square, ((0, 0), (0, pad), (0, 0)))
    send = jnp.stack([padded_square, look_wide], axis=1).reshape(
        tensor_count, piece, look_wide.shape[2]
    )
    held = lax.all_to_all(send, "tensor", split_axis=0, concat_axis=0, tiled=True)
    rows = held.reshape(tensor_count * piece, held.shape[2])

    gram = lax.psum(gram_of(rows), "shard")
    columns = gram.shape[0]
    eye = jnp.eye(columns, dtype=jnp.float32)
    total = jnp.sum(gram * eye)
    denom = jnp.sqrt(total) + epsilon
    current = rows / denom
    gram = gram / (denom * denom)
    for iteration in range(ITERS):
        square_gram = dot(gram, gram)
        mixer = coef_b * gram + coef_c * square_gram
        current = coef_a * current + dot(current, mixer)
        if iteration + 1 < ITERS:
            full = mixer + coef_a * eye
            gram = dot(full, dot(gram, full))

    is_square = member % 2 == 0
    scale = jnp.where(
        is_square, jnp.float32(math.sqrt(D)), jnp.float32(math.sqrt(FF))
    )
    update = scale * current
    gathered = lax.all_gather(update[None], "tensor", axis=0, tiled=True)
    gathered = gathered.reshape(count_square, 2, tensor_count, piece, update.shape[1])
    update_square = gathered[:, 0, :, : piece - pad].reshape(
        count_square, tensor_count * (piece - pad), update.shape[1]
    )
    update_wide = gathered[:, 1].reshape(
        count_wide, tensor_count * piece, update.shape[1]
    )
    return (
        update_square,
        update_wide,
        new_square.reshape(moment_square.shape),
        new_wide.reshape(moment_wide.shape),
    )


def solution(mesh):
    return jax.shard_map(
        shards,
        mesh=mesh,
        in_specs=(
            P(None, "shard", None),
            P(None, "shard", None),
            P(None, ("shard", "tensor")),
            P(None, ("shard", "tensor")),
        ),
        out_specs=(
            P(None, "shard", None),
            P(None, "shard", None),
            P(None, ("shard", "tensor")),
            P(None, ("shard", "tensor")),
        ),
        check_vma=False,
    )
```

```python
import math

import jax
import jax.numpy as jnp
from jax import lax
from jax.sharding import PartitionSpec as P

D = 768
FF = 2048
ITERS = 3


coef_a = 3.4445
coef_b = -4.775
coef_c = 2.0315
momentum_decay = 0.95
epsilon = 1e-07

PRECISION = lax.Precision.HIGH


def dot(x, y):
    return jnp.dot(x, y, precision=PRECISION, preferred_element_type=jnp.float32)


def gram_of(rows):
    return lax.dot_general(
        rows,
        rows,
        (((0,), (0,)), ((), ())),
        precision=PRECISION,
        preferred_element_type=jnp.float32,
    )


def own_rows(grad, member, tensor_count):
    row_piece = grad.shape[1] // tensor_count
    return lax.dynamic_slice_in_dim(grad, member * row_piece, row_piece, 1)


def shards(grad_square, grad_wide, moment_square, moment_wide):
    tensor_count = lax.axis_size("tensor")
    member = lax.axis_index("tensor")
    count_square, count_wide = grad_square.shape[0], grad_wide.shape[0]
    assert count_square == count_wide and 2 * count_square == tensor_count
    flat_square = own_rows(grad_square, member, tensor_count).astype(jnp.float32)
    flat_wide = own_rows(grad_wide, member, tensor_count).astype(jnp.float32)
    new_square = momentum_decay * moment_square.reshape(flat_square.shape) + flat_square
    new_wide = momentum_decay * moment_wide.reshape(flat_wide.shape) + flat_wide
    look_square = flat_square + momentum_decay * new_square
    look_wide = flat_wide + momentum_decay * new_wide

    piece = look_wide.shape[1]
    pad = piece - look_square.shape[1]
    padded_square = jnp.pad(look_square, ((0, 0), (0, pad), (0, 0)))
    send = jnp.stack([padded_square, look_wide], axis=1).reshape(
        tensor_count, piece, look_wide.shape[2]
    )
    held = lax.all_to_all(send, "tensor", split_axis=0, concat_axis=0, tiled=True)
    rows = held.reshape(tensor_count * piece, held.shape[2])

    gram = lax.psum(gram_of(rows), "shard")
    columns = gram.shape[0]
    eye = jnp.eye(columns, dtype=jnp.float32)
    total = jnp.sum(gram * eye)
    denom = jnp.sqrt(total) + epsilon
    current = rows / denom
    gram = gram / (denom * denom)
    for iteration in range(ITERS):
        square_gram = dot(gram, gram)
        mixer = coef_b * gram + coef_c * square_gram
        current = coef_a * current + dot(current, mixer)
        if iteration + 1 < ITERS:
            full = mixer + coef_a * eye
            gram = dot(full, dot(gram, full))

    is_square = member % 2 == 0
    scale = jnp.where(
        is_square, jnp.float32(math.sqrt(D)), jnp.float32(math.sqrt(FF))
    )
    update = scale * current
    gathered = lax.all_gather(update[None], "tensor", axis=0, tiled=True)
    gathered = gathered.reshape(count_square, 2, tensor_count, piece, update.shape[1])
    update_square = gathered[:, 0, :, : piece - pad].reshape(
        count_square, tensor_count * (piece - pad), update.shape[1]
    )
    update_wide = gathered[:, 1].reshape(
        count_wide, tensor_count * piece, update.shape[1]
    )
    return (
        update_square,
        update_wide,
        new_square.reshape(moment_square.shape),
        new_wide.reshape(moment_wide.shape),
    )


def solution(mesh):
    return jax.shard_map(
        shards,
        mesh=mesh,
        in_specs=(
            P(None, "shard", None),
            P(None, "shard", None),
            P(None, ("shard", "tensor")),
            P(None, ("shard", "tensor")),
        ),
        out_specs=(
            P(None, "shard", None),
            P(None, "shard", None),
            P(None, ("shard", "tensor")),
            P(None, ("shard", "tensor")),
        ),
        check_vma=False,
    )
```

```python
import math

import jax
import jax.numpy as jnp
from jax import lax
from jax.sharding import PartitionSpec as P

D = 768
FF = 2048
ITERS = 3


coef_a = 3.4445
coef_b = -4.775
coef_c = 2.0315
momentum_decay = 0.95
epsilon = 1e-07

PRECISION = lax.Precision.HIGH


def dot(x, y):
    return jnp.dot(x, y, precision=PRECISION, preferred_element_type=jnp.float32)


def gram_of(rows):
    return lax.dot_general(
        rows,
        rows,
        (((0,), (0,)), ((), ())),
        precision=PRECISION,
        preferred_element_type=jnp.float32,
    )


def own_rows(grad, member, tensor_count):
    row_piece = grad.shape[1] // tensor_count
    return lax.dynamic_slice_in_dim(grad, member * row_piece, row_piece, 1)


def shards(grad_square, grad_wide, moment_square, moment_wide):
    tensor_count = lax.axis_size("tensor")
    member = lax.axis_index("tensor")
    count_square, count_wide = grad_square.shape[0], grad_wide.shape[0]
    assert count_square == count_wide and 2 * count_square == tensor_count
    flat_square = own_rows(grad_square, member, tensor_count).astype(jnp.float32)
    flat_wide = own_rows(grad_wide, member, tensor_count).astype(jnp.float32)
    new_square = momentum_decay * moment_square.reshape(flat_square.shape) + flat_square
    new_wide = momentum_decay * moment_wide.reshape(flat_wide.shape) + flat_wide
    look_square = flat_square + momentum_decay * new_square
    look_wide = flat_wide + momentum_decay * new_wide

    piece = look_wide.shape[1]
    pad = piece - look_square.shape[1]
    padded_square = jnp.pad(look_square, ((0, 0), (0, pad), (0, 0)))
    send = jnp.stack([padded_square, look_wide], axis=1).reshape(
        tensor_count, piece, look_wide.shape[2]
    )
    held = lax.all_to_all(send, "tensor", split_axis=0, concat_axis=0, tiled=True)
    rows = held.reshape(tensor_count * piece, held.shape[2])

    gram = lax.psum(gram_of(rows), "shard")
    columns = gram.shape[0]
    eye = jnp.eye(columns, dtype=jnp.float32)
    total = jnp.sum(gram * eye)
    denom = jnp.sqrt(total) + epsilon
    current = rows / denom
    gram = gram / (denom * denom)
    for iteration in range(ITERS):
        square_gram = dot(gram, gram)
        mixer = coef_b * gram + coef_c * square_gram
        current = coef_a * current + dot(current, mixer)
        if iteration + 1 < ITERS:
            full = mixer + coef_a * eye
            gram = dot(full, dot(gram, full))

    is_square = member % 2 == 0
    scale = jnp.where(
        is_square, jnp.float32(math.sqrt(D)), jnp.float32(math.sqrt(FF))
    )
    update = scale * current
    square_piece = piece - pad
    square_rows = update.reshape(tensor_count, piece, -1)[:, :square_piece]
    square_rows = square_rows.reshape(tensor_count * square_piece, -1)
    square_half = square_rows.shape[0] // 2
    wide_half = update.shape[0] // 2
    pairs = count_square
    to_odd = [(2 * j, 2 * j + 1) for j in range(pairs)]
    to_even = [(2 * j + 1, 2 * j) for j in range(pairs)]
    got_square = lax.ppermute(square_rows[square_half:], "tensor", to_odd)
    got_wide = lax.ppermute(update[:wide_half], "tensor", to_even)
    mine_square = jnp.where(is_square, square_rows[:square_half], got_square)
    mine_wide = jnp.where(is_square, got_wide, update[wide_half:])
    update_square = lax.all_gather(mine_square, "tensor", axis=0, tiled=True)
    update_wide = lax.all_gather(mine_wide, "tensor", axis=0, tiled=True)
    update_square = update_square.reshape(count_square, -1, update.shape[1])
    update_wide = update_wide.reshape(count_wide, -1, update.shape[1])
    return (
        update_square,
        update_wide,
        new_square.reshape(moment_square.shape),
        new_wide.reshape(moment_wide.shape),
    )


def solution(mesh):
    return jax.shard_map(
        shards,
        mesh=mesh,
        in_specs=(
            P(None, "shard", None),
            P(None, "shard", None),
            P(None, ("shard", "tensor")),
            P(None, ("shard", "tensor")),
        ),
        out_specs=(
            P(None, "shard", None),
            P(None, "shard", None),
            P(None, ("shard", "tensor")),
            P(None, ("shard", "tensor")),
        ),
        check_vma=False,
    )
```

```python
import math

import jax
import jax.numpy as jnp
from jax import lax
from jax.sharding import PartitionSpec as P

D = 768
FF = 2048
ITERS = 3


coef_a = 3.4445
coef_b = -4.775
coef_c = 2.0315
momentum_decay = 0.95
epsilon = 1e-07

PRECISION = lax.Precision.HIGH


def dot(x, y):
    return jnp.dot(x, y, precision=PRECISION, preferred_element_type=jnp.float32)


def gram_of(rows):
    return lax.dot_general(
        rows,
        rows,
        (((0,), (0,)), ((), ())),
        precision=PRECISION,
        preferred_element_type=jnp.float32,
    )


def own_rows(grad, member, tensor_count):
    row_piece = grad.shape[1] // tensor_count
    return lax.dynamic_slice_in_dim(grad, member * row_piece, row_piece, 1)


def shards(grad_square, grad_wide, moment_square, moment_wide):
    tensor_count = lax.axis_size("tensor")
    member = lax.axis_index("tensor")
    count_square, count_wide = grad_square.shape[0], grad_wide.shape[0]
    assert count_square == count_wide and 2 * count_square == tensor_count
    flat_square = own_rows(grad_square, member, tensor_count).astype(jnp.float32)
    flat_wide = own_rows(grad_wide, member, tensor_count).astype(jnp.float32)
    new_square = momentum_decay * moment_square.reshape(flat_square.shape) + flat_square
    new_wide = momentum_decay * moment_wide.reshape(flat_wide.shape) + flat_wide
    look_square = flat_square + momentum_decay * new_square
    look_wide = flat_wide + momentum_decay * new_wide

    piece = look_wide.shape[1]
    pad = piece - look_square.shape[1]
    padded_square = jnp.pad(look_square, ((0, 0), (0, pad), (0, 0)))
    send = jnp.stack([padded_square, look_wide], axis=1).reshape(
        tensor_count, piece, look_wide.shape[2]
    )
    held = lax.all_to_all(send, "tensor", split_axis=0, concat_axis=0, tiled=True)
    rows = held.reshape(tensor_count * piece, held.shape[2])

    part = gram_of(rows)
    columns = part.shape[0]
    half = columns // 2
    assert 2 * half == columns and half % 8 == 0
    row_id = lax.broadcasted_iota(jnp.int32, (half, half), 0)
    col_id = lax.broadcasted_iota(jnp.int32, (half, half), 1)
    upper = col_id >= row_id
    on_diagonal = col_id == row_id
    corner = part[half:, half:]
    folded = jnp.where(upper, part[:half, :half], corner)
    corner_diagonal = jnp.sum(jnp.where(on_diagonal, corner, 0.0), axis=0)
    tail = jnp.zeros((8, half), jnp.float32).at[0].set(corner_diagonal)
    packed = jnp.concatenate([part[:half, half:], folded, tail], axis=0)
    packed = lax.psum(packed, "shard")
    side = packed[:half]
    folded = packed[half:columns]
    corner_diagonal = packed[columns]
    flipped = folded.T
    top_left = jnp.where(upper, folded, flipped)
    bottom_right = jnp.where(
        on_diagonal, corner_diagonal[None, :], jnp.where(upper, flipped, folded)
    )
    gram = jnp.concatenate(
        [
            jnp.concatenate([top_left, side], axis=1),
            jnp.concatenate([side.T, bottom_right], axis=1),
        ],
        axis=0,
    )
    total = jnp.sum(jnp.where(on_diagonal, folded, 0.0)) + jnp.sum(corner_diagonal)
    eye = jnp.eye(columns, dtype=jnp.float32)
    denom = jnp.sqrt(total) + epsilon
    current = rows / denom
    gram = gram / (denom * denom)
    for iteration in range(ITERS):
        square_gram = dot(gram, gram)
        mixer = coef_b * gram + coef_c * square_gram
        current = coef_a * current + dot(current, mixer)
        if iteration + 1 < ITERS:
            full = mixer + coef_a * eye
            gram = dot(full, dot(gram, full))

    is_square = member % 2 == 0
    scale = jnp.where(
        is_square, jnp.float32(math.sqrt(D)), jnp.float32(math.sqrt(FF))
    )
    update = scale * current
    gathered = lax.all_gather(update[None], "tensor", axis=0, tiled=True)
    gathered = gathered.reshape(count_square, 2, tensor_count, piece, update.shape[1])
    update_square = gathered[:, 0, :, : piece - pad].reshape(
        count_square, tensor_count * (piece - pad), update.shape[1]
    )
    update_wide = gathered[:, 1].reshape(
        count_wide, tensor_count * piece, update.shape[1]
    )
    return (
        update_square,
        update_wide,
        new_square.reshape(moment_square.shape),
        new_wide.reshape(moment_wide.shape),
    )


def solution(mesh):
    return jax.shard_map(
        shards,
        mesh=mesh,
        in_specs=(
            P(None, "shard", None),
            P(None, "shard", None),
            P(None, ("shard", "tensor")),
            P(None, ("shard", "tensor")),
        ),
        out_specs=(
            P(None, "shard", None),
            P(None, "shard", None),
            P(None, ("shard", "tensor")),
            P(None, ("shard", "tensor")),
        ),
        check_vma=False,
    )
```

```python
import math

import jax
import jax.numpy as jnp
from jax import lax
from jax.sharding import PartitionSpec as P

D = 768
FF = 2048
ITERS = 3


coef_a = 3.4445
coef_b = -4.775
coef_c = 2.0315
momentum_decay = 0.95
epsilon = 1e-07

PRECISION = lax.Precision.HIGH


def dot(x, y):
    return jnp.dot(x, y, precision=PRECISION, preferred_element_type=jnp.float32)


def gram_of(rows):
    return lax.dot_general(
        rows,
        rows,
        (((0,), (0,)), ((), ())),
        precision=PRECISION,
        preferred_element_type=jnp.float32,
    )


def own_rows(grad, member, tensor_count):
    row_piece = grad.shape[1] // tensor_count
    return lax.dynamic_slice_in_dim(grad, member * row_piece, row_piece, 1)


def shards(grad_square, grad_wide, moment_square, moment_wide):
    tensor_count = lax.axis_size("tensor")
    member = lax.axis_index("tensor")
    count_square, count_wide = grad_square.shape[0], grad_wide.shape[0]
    assert count_square == count_wide and 2 * count_square == tensor_count
    flat_square = own_rows(grad_square, member, tensor_count).astype(jnp.float32)
    flat_wide = own_rows(grad_wide, member, tensor_count).astype(jnp.float32)
    new_square = momentum_decay * moment_square.reshape(flat_square.shape) + flat_square
    new_wide = momentum_decay * moment_wide.reshape(flat_wide.shape) + flat_wide
    look_square = flat_square + momentum_decay * new_square
    look_wide = flat_wide + momentum_decay * new_wide

    piece = look_wide.shape[1]
    pad = piece - look_square.shape[1]
    padded_square = jnp.pad(look_square, ((0, 0), (0, pad), (0, 0)))
    send = jnp.stack([padded_square, look_wide], axis=1).reshape(
        tensor_count, piece, look_wide.shape[2]
    )
    held = lax.all_to_all(send, "tensor", split_axis=0, concat_axis=0, tiled=True)
    rows = held.reshape(tensor_count * piece, held.shape[2])

    gram = lax.psum(gram_of(rows), "shard")
    columns = gram.shape[0]
    eye = jnp.eye(columns, dtype=jnp.float32)
    total = jnp.sum(gram * eye)
    denom = jnp.sqrt(total) + epsilon
    current = rows / denom
    shrink = 1.0 / (denom * denom)
    for iteration in range(ITERS):
        square_gram = dot(gram, gram)
        if iteration == 0:
            mixer = (coef_b * shrink) * gram + (coef_c * shrink * shrink) * square_gram
        else:
            mixer = coef_b * gram + coef_c * square_gram
        current = coef_a * current + dot(current, mixer)
        if iteration + 1 < ITERS:
            full = mixer + coef_a * eye
            gram = dot(full, dot(gram, full))
            if iteration == 0:
                gram = shrink * gram

    is_square = member % 2 == 0
    scale = jnp.where(
        is_square, jnp.float32(math.sqrt(D)), jnp.float32(math.sqrt(FF))
    )
    update = scale * current
    square_piece = piece - pad
    square_rows = update.reshape(tensor_count, piece, -1)[:, :square_piece]
    square_rows = square_rows.reshape(tensor_count * square_piece, -1)
    wide_rows = update.shape[0]
    chunk = (square_rows.shape[0] + wide_rows) // 2
    assert 2 * chunk == square_rows.shape[0] + wide_rows
    to_even = [(2 * j + 1, 2 * j) for j in range(count_square)]
    handed = lax.ppermute(update[chunk:], "tensor", to_even)
    mine = jnp.where(
        is_square, jnp.concatenate([square_rows, handed], axis=0), update[:chunk]
    )
    gathered = lax.all_gather(mine, "tensor", axis=0, tiled=True)
    gathered = gathered.reshape(count_square, 2, chunk, update.shape[1])
    update_square = gathered[:, 0, : square_rows.shape[0]]
    update_wide = jnp.concatenate(
        [gathered[:, 1], gathered[:, 0, square_rows.shape[0]:]], axis=1
    )
    return (
        update_square,
        update_wide,
        new_square.reshape(moment_square.shape),
        new_wide.reshape(moment_wide.shape),
    )


def solution(mesh):
    return jax.shard_map(
        shards,
        mesh=mesh,
        in_specs=(
            P(None, "shard", None),
            P(None, "shard", None),
            P(None, ("shard", "tensor")),
            P(None, ("shard", "tensor")),
        ),
        out_specs=(
            P(None, "shard", None),
            P(None, "shard", None),
            P(None, ("shard", "tensor")),
            P(None, ("shard", "tensor")),
        ),
        check_vma=False,
    )
```

```python
import math

import jax
import jax.numpy as jnp
from jax import lax
from jax.sharding import PartitionSpec as P

D = 768
FF = 2048
ITERS = 3


coef_a = 3.4445
coef_b = -4.775
coef_c = 2.0315
momentum_decay = 0.95
epsilon = 1e-07

PRECISION = lax.Precision.HIGH


def dot(x, y):
    return jnp.dot(x, y, precision=PRECISION, preferred_element_type=jnp.float32)


def gram_of(rows):
    return lax.dot_general(
        rows,
        rows,
        (((0,), (0,)), ((), ())),
        precision=PRECISION,
        preferred_element_type=jnp.float32,
    )


def own_rows(grad, member, tensor_count):
    row_piece = grad.shape[1] // tensor_count
    return lax.dynamic_slice_in_dim(grad, member * row_piece, row_piece, 1)


def shards(grad_square, grad_wide, moment_square, moment_wide):
    tensor_count = lax.axis_size("tensor")
    member = lax.axis_index("tensor")
    count_square, count_wide = grad_square.shape[0], grad_wide.shape[0]
    assert count_square == count_wide and 2 * count_square == tensor_count
    flat_square = own_rows(grad_square, member, tensor_count).astype(jnp.float32)
    flat_wide = own_rows(grad_wide, member, tensor_count).astype(jnp.float32)
    new_square = momentum_decay * moment_square.reshape(flat_square.shape) + flat_square
    new_wide = momentum_decay * moment_wide.reshape(flat_wide.shape) + flat_wide
    look_square = flat_square + momentum_decay * new_square
    look_wide = flat_wide + momentum_decay * new_wide

    piece = look_wide.shape[1]
    pad = piece - look_square.shape[1]
    padded_square = jnp.pad(look_square, ((0, 0), (0, pad), (0, 0)))
    send = jnp.stack([look_wide, padded_square], axis=1).reshape(
        tensor_count, piece, look_wide.shape[2]
    )
    held = lax.all_to_all(send, "tensor", split_axis=0, concat_axis=0, tiled=True)
    rows = held.reshape(tensor_count * piece, held.shape[2])

    gram = lax.psum(gram_of(rows), "shard")
    columns = gram.shape[0]
    eye = jnp.eye(columns, dtype=jnp.float32)
    total = jnp.sum(gram * eye)
    denom = jnp.sqrt(total) + epsilon
    current = rows / denom
    shrink = 1.0 / (denom * denom)
    for iteration in range(ITERS):
        square_gram = dot(gram, gram)
        if iteration == 0:
            mixer = (coef_b * shrink) * gram + (coef_c * shrink * shrink) * square_gram
        else:
            mixer = coef_b * gram + coef_c * square_gram
        current = coef_a * current + dot(current, mixer)
        if iteration + 1 < ITERS:
            full = mixer + coef_a * eye
            gram = dot(full, dot(gram, full))
            if iteration == 0:
                gram = shrink * gram

    is_square = member % 2 == 1
    scale = jnp.where(
        is_square, jnp.float32(math.sqrt(D)), jnp.float32(math.sqrt(FF))
    )
    update = scale * current
    square_piece = piece - pad
    square_rows = update.reshape(tensor_count, piece, -1)[:, :square_piece]
    square_rows = square_rows.reshape(tensor_count * square_piece, -1)
    wide_rows = update.shape[0]
    chunk = (square_rows.shape[0] + wide_rows) // 2
    assert 2 * chunk == square_rows.shape[0] + wide_rows
    to_odd = [(2 * j, 2 * j + 1) for j in range(count_square)]
    handed = lax.ppermute(update[chunk:], "tensor", to_odd)
    mine = jnp.where(
        is_square, jnp.concatenate([handed, square_rows], axis=0), update[:chunk]
    )
    gathered = lax.all_gather(mine, "tensor", axis=0, tiled=True)
    gathered = gathered.reshape(count_square, 2 * chunk, update.shape[1])
    update_wide = gathered[:, :wide_rows]
    update_square = gathered[:, wide_rows:]
    return (
        update_square,
        update_wide,
        new_square.reshape(moment_square.shape),
        new_wide.reshape(moment_wide.shape),
    )


def solution(mesh):
    return jax.shard_map(
        shards,
        mesh=mesh,
        in_specs=(
            P(None, "shard", None),
            P(None, "shard", None),
            P(None, ("shard", "tensor")),
            P(None, ("shard", "tensor")),
        ),
        out_specs=(
            P(None, "shard", None),
            P(None, "shard", None),
            P(None, ("shard", "tensor")),
            P(None, ("shard", "tensor")),
        ),
        check_vma=False,
    )
```

```python
import math

import jax
import jax.numpy as jnp
from jax import lax
from jax.sharding import PartitionSpec as P

D = 768
FF = 2048
ITERS = 3


coef_a = 3.4445
coef_b = -4.775
coef_c = 2.0315
momentum_decay = 0.95
epsilon = 1e-07

PRECISION = lax.Precision.HIGH


def dot(x, y):
    return jnp.dot(x, y, precision=PRECISION, preferred_element_type=jnp.float32)


def gram_of(rows):
    return lax.dot_general(
        rows,
        rows,
        (((0,), (0,)), ((), ())),
        precision=PRECISION,
        preferred_element_type=jnp.float32,
    )


def halving_psum(values, axis):
    count = lax.axis_size(axis)
    me = lax.axis_index(axis)
    steps = count.bit_length() - 1
    assert 1 << steps == count and values.shape[0] % count == 0
    held = values
    for level in range(steps):
        step = 1 << level
        half = held.shape[0] // 2
        upper = (me // step) % 2
        keep = lax.dynamic_slice_in_dim(held, upper * half, half, 0)
        give = lax.dynamic_slice_in_dim(held, (1 - upper) * half, half, 0)
        pairs = [(i, i ^ step) for i in range(count)]
        held = keep + lax.ppermute(give, axis, pairs)
    for level in reversed(range(steps)):
        step = 1 << level
        upper = (me // step) % 2
        pairs = [(i, i ^ step) for i in range(count)]
        got = lax.ppermute(held, axis, pairs)
        held = jnp.where(
            upper == 1,
            jnp.concatenate([got, held], axis=0),
            jnp.concatenate([held, got], axis=0),
        )
    return held


def own_rows(grad, member, tensor_count):
    row_piece = grad.shape[1] // tensor_count
    return lax.dynamic_slice_in_dim(grad, member * row_piece, row_piece, 1)


def shards(grad_square, grad_wide, moment_square, moment_wide):
    tensor_count = lax.axis_size("tensor")
    member = lax.axis_index("tensor")
    count_square, count_wide = grad_square.shape[0], grad_wide.shape[0]
    assert count_square == count_wide and 2 * count_square == tensor_count
    flat_square = own_rows(grad_square, member, tensor_count).astype(jnp.float32)
    flat_wide = own_rows(grad_wide, member, tensor_count).astype(jnp.float32)
    new_square = momentum_decay * moment_square.reshape(flat_square.shape) + flat_square
    new_wide = momentum_decay * moment_wide.reshape(flat_wide.shape) + flat_wide
    look_square = flat_square + momentum_decay * new_square
    look_wide = flat_wide + momentum_decay * new_wide

    piece = look_wide.shape[1]
    pad = piece - look_square.shape[1]
    padded_square = jnp.pad(look_square, ((0, 0), (0, pad), (0, 0)))
    send = jnp.stack([look_wide, padded_square], axis=1).reshape(
        tensor_count, piece, look_wide.shape[2]
    )
    held = lax.all_to_all(send, "tensor", split_axis=0, concat_axis=0, tiled=True)
    rows = held.reshape(tensor_count * piece, held.shape[2])

    gram = halving_psum(gram_of(rows), "shard")
    columns = gram.shape[0]
    eye = jnp.eye(columns, dtype=jnp.float32)
    total = jnp.sum(gram * eye)
    denom = jnp.sqrt(total) + epsilon
    current = rows / denom
    shrink = 1.0 / (denom * denom)
    for iteration in range(ITERS):
        square_gram = dot(gram, gram)
        if iteration == 0:
            mixer = (coef_b * shrink) * gram + (coef_c * shrink * shrink) * square_gram
        else:
            mixer = coef_b * gram + coef_c * square_gram
        current = coef_a * current + dot(current, mixer)
        if iteration + 1 < ITERS:
            full = mixer + coef_a * eye
            gram = dot(full, dot(gram, full))
            if iteration == 0:
                gram = shrink * gram

    is_square = member % 2 == 1
    scale = jnp.where(
        is_square, jnp.float32(math.sqrt(D)), jnp.float32(math.sqrt(FF))
    )
    update = scale * current
    square_piece = piece - pad
    square_rows = update.reshape(tensor_count, piece, -1)[:, :square_piece]
    square_rows = square_rows.reshape(tensor_count * square_piece, -1)
    wide_rows = update.shape[0]
    chunk = (square_rows.shape[0] + wide_rows) // 2
    assert 2 * chunk == square_rows.shape[0] + wide_rows
    to_odd = [(2 * j, 2 * j + 1) for j in range(count_square)]
    handed = lax.ppermute(update[chunk:], "tensor", to_odd)
    mine = jnp.where(
        is_square, jnp.concatenate([handed, square_rows], axis=0), update[:chunk]
    )
    gathered = lax.all_gather(mine, "tensor", axis=0, tiled=True)
    gathered = gathered.reshape(count_square, 2 * chunk, update.shape[1])
    update_wide = gathered[:, :wide_rows]
    update_square = gathered[:, wide_rows:]
    return (
        update_square,
        update_wide,
        new_square.reshape(moment_square.shape),
        new_wide.reshape(moment_wide.shape),
    )


def solution(mesh):
    return jax.shard_map(
        shards,
        mesh=mesh,
        in_specs=(
            P(None, "shard", None),
            P(None, "shard", None),
            P(None, ("shard", "tensor")),
            P(None, ("shard", "tensor")),
        ),
        out_specs=(
            P(None, "shard", None),
            P(None, "shard", None),
            P(None, ("shard", "tensor")),
            P(None, ("shard", "tensor")),
        ),
        check_vma=False,
    )
```

```python
import math

import jax
import jax.numpy as jnp
from jax import lax
from jax.sharding import PartitionSpec as P

D = 768
FF = 2048
ITERS = 3


coef_a = 3.4445
coef_b = -4.775
coef_c = 2.0315
momentum_decay = 0.95
epsilon = 1e-07

PRECISION = lax.Precision.HIGH


def dot(x, y):
    return jnp.dot(x, y, precision=PRECISION, preferred_element_type=jnp.float32)


def gram_of(rows):
    return lax.dot_general(
        rows,
        rows,
        (((0,), (0,)), ((), ())),
        precision=PRECISION,
        preferred_element_type=jnp.float32,
    )


def own_rows(grad, member, tensor_count):
    row_piece = grad.shape[1] // tensor_count
    return lax.dynamic_slice_in_dim(grad, member * row_piece, row_piece, 1)


def shards(grad_square, grad_wide, moment_square, moment_wide):
    tensor_count = lax.axis_size("tensor")
    member = lax.axis_index("tensor")
    count_square, count_wide = grad_square.shape[0], grad_wide.shape[0]
    assert count_square == count_wide and 2 * count_square == tensor_count
    flat_square = own_rows(grad_square, member, tensor_count).astype(jnp.float32)
    flat_wide = own_rows(grad_wide, member, tensor_count).astype(jnp.float32)
    new_square = momentum_decay * moment_square.reshape(flat_square.shape) + flat_square
    new_wide = momentum_decay * moment_wide.reshape(flat_wide.shape) + flat_wide
    look_square = flat_square + momentum_decay * new_square
    look_wide = flat_wide + momentum_decay * new_wide

    piece = look_wide.shape[1]
    pad = piece - look_square.shape[1]
    padded_square = jnp.pad(look_square, ((0, 0), (0, pad), (0, 0)))
    send = jnp.stack([look_wide, padded_square], axis=1).reshape(
        tensor_count, piece, look_wide.shape[2]
    )
    held = lax.all_to_all(send, "tensor", split_axis=0, concat_axis=0, tiled=True)
    rows = held.reshape(tensor_count * piece, held.shape[2])

    gram = lax.psum(gram_of(rows), "shard")
    columns = gram.shape[0]
    eye = jnp.eye(columns, dtype=jnp.float32)
    total = jnp.sum(gram * eye)
    denom = jnp.sqrt(total) + epsilon
    current = rows / denom
    shrink = 1.0 / (denom * denom)
    for iteration in range(ITERS - 1):
        square_gram = dot(gram, gram)
        if iteration == 0:
            mixer = (coef_b * shrink) * gram + (coef_c * shrink * shrink) * square_gram
        else:
            mixer = coef_b * gram + coef_c * square_gram
        current = coef_a * current + dot(current, mixer)
        full = mixer + coef_a * eye
        gram = dot(full, dot(gram, full))
        if iteration == 0:
            gram = shrink * gram
    if ITERS == 1:
        gram = shrink * gram
    side = dot(current, gram)
    current = coef_a * current + (coef_b * side + coef_c * dot(side, gram))

    is_square = member % 2 == 1
    scale = jnp.where(
        is_square, jnp.float32(math.sqrt(D)), jnp.float32(math.sqrt(FF))
    )
    update = scale * current
    square_piece = piece - pad
    square_rows = update.reshape(tensor_count, piece, -1)[:, :square_piece]
    square_rows = square_rows.reshape(tensor_count * square_piece, -1)
    wide_rows = update.shape[0]
    chunk = (square_rows.shape[0] + wide_rows) // 2
    assert 2 * chunk == square_rows.shape[0] + wide_rows
    to_odd = [(2 * j, 2 * j + 1) for j in range(count_square)]
    handed = lax.ppermute(update[chunk:], "tensor", to_odd)
    mine = jnp.where(
        is_square, jnp.concatenate([handed, square_rows], axis=0), update[:chunk]
    )
    gathered = lax.all_gather(mine, "tensor", axis=0, tiled=True)
    gathered = gathered.reshape(count_square, 2 * chunk, update.shape[1])
    update_wide = gathered[:, :wide_rows]
    update_square = gathered[:, wide_rows:]
    return (
        update_square,
        update_wide,
        new_square.reshape(moment_square.shape),
        new_wide.reshape(moment_wide.shape),
    )


def solution(mesh):
    return jax.shard_map(
        shards,
        mesh=mesh,
        in_specs=(
            P(None, "shard", None),
            P(None, "shard", None),
            P(None, ("shard", "tensor")),
            P(None, ("shard", "tensor")),
        ),
        out_specs=(
            P(None, "shard", None),
            P(None, "shard", None),
            P(None, ("shard", "tensor")),
            P(None, ("shard", "tensor")),
        ),
        check_vma=False,
    )
```

```python
import math

import jax
import jax.numpy as jnp
from jax import lax
from jax.sharding import PartitionSpec as P

D = 768
FF = 2048
ITERS = 3


coef_a = 3.4445
coef_b = -4.775
coef_c = 2.0315
momentum_decay = 0.95
epsilon = 1e-07

PRECISION = lax.Precision.HIGH


def dot(x, y):
    return jnp.dot(x, y, precision=PRECISION, preferred_element_type=jnp.float32)


def gram_of(rows):
    return lax.dot_general(
        rows,
        rows,
        (((0,), (0,)), ((), ())),
        precision=PRECISION,
        preferred_element_type=jnp.float32,
    )


def own_rows(grad, member, tensor_count):
    row_piece = grad.shape[1] // tensor_count
    return lax.dynamic_slice_in_dim(grad, member * row_piece, row_piece, 1)


def shards(grad_square, grad_wide, moment_square, moment_wide):
    tensor_count = lax.axis_size("tensor")
    member = lax.axis_index("tensor")
    count_square, count_wide = grad_square.shape[0], grad_wide.shape[0]
    assert count_square == count_wide and 2 * count_square == tensor_count
    flat_square = own_rows(grad_square, member, tensor_count).astype(jnp.float32)
    flat_wide = own_rows(grad_wide, member, tensor_count).astype(jnp.float32)
    new_square = momentum_decay * moment_square.reshape(flat_square.shape) + flat_square
    new_wide = momentum_decay * moment_wide.reshape(flat_wide.shape) + flat_wide
    look_square = flat_square + momentum_decay * new_square
    look_wide = flat_wide + momentum_decay * new_wide

    piece = look_wide.shape[1]
    pad = piece - look_square.shape[1]
    padded_square = jnp.pad(look_square, ((0, 0), (0, pad), (0, 0)))
    send = jnp.stack([look_wide, padded_square], axis=1).reshape(
        tensor_count, piece, look_wide.shape[2]
    )
    held = lax.all_to_all(send, "tensor", split_axis=0, concat_axis=0, tiled=True)
    rows = held.reshape(tensor_count * piece, held.shape[2])

    gram = lax.psum(gram_of(rows), "shard")
    columns = gram.shape[0]
    eye = jnp.eye(columns, dtype=jnp.float32)
    total = jnp.sum(gram * eye)
    denom = jnp.sqrt(total) + epsilon
    current = rows / denom
    gram = lax.optimization_barrier(gram / (denom * denom))
    for iteration in range(ITERS - 1):
        square_gram = dot(gram, gram)
        mixer = coef_b * gram + coef_c * square_gram
        current = coef_a * current + dot(current, mixer)
        full = mixer + coef_a * eye
        gram = dot(full, dot(gram, full))
    is_square = member % 2 == 1
    scale = jnp.where(
        is_square, jnp.float32(math.sqrt(D)), jnp.float32(math.sqrt(FF))
    )

    def finish(block):
        side = dot(block, gram)
        return scale * (coef_a * block + (coef_b * side + coef_c * dot(side, gram)))

    square_piece = piece - pad
    split = (current.shape[0] + (piece - pad) * tensor_count) // 2
    head, tail = finish(current[:split]), finish(current[split:])
    update = jnp.concatenate([head, tail], axis=0)
    square_rows = update.reshape(tensor_count, piece, -1)[:, :square_piece]
    square_rows = square_rows.reshape(tensor_count * square_piece, -1)
    wide_rows = update.shape[0]
    chunk = (square_rows.shape[0] + wide_rows) // 2
    assert 2 * chunk == square_rows.shape[0] + wide_rows and chunk == split
    to_odd = [(2 * j, 2 * j + 1) for j in range(count_square)]
    handed = lax.ppermute(tail, "tensor", to_odd)
    mine = jnp.where(
        is_square, jnp.concatenate([handed, square_rows], axis=0), head
    )
    gathered = lax.all_gather(mine, "tensor", axis=0, tiled=True)
    gathered = gathered.reshape(count_square, 2 * chunk, update.shape[1])
    update_wide = gathered[:, :wide_rows]
    update_square = gathered[:, wide_rows:]
    return (
        update_square,
        update_wide,
        new_square.reshape(moment_square.shape),
        new_wide.reshape(moment_wide.shape),
    )


def solution(mesh):
    return jax.shard_map(
        shards,
        mesh=mesh,
        in_specs=(
            P(None, "shard", None),
            P(None, "shard", None),
            P(None, ("shard", "tensor")),
            P(None, ("shard", "tensor")),
        ),
        out_specs=(
            P(None, "shard", None),
            P(None, "shard", None),
            P(None, ("shard", "tensor")),
            P(None, ("shard", "tensor")),
        ),
        check_vma=False,
    )
```

```python
import math

import jax
import jax.numpy as jnp
from jax import lax
from jax.sharding import PartitionSpec as P

D = 768
FF = 2048
ITERS = 3


coef_a = 3.4445
coef_b = -4.775
coef_c = 2.0315
momentum_decay = 0.95
epsilon = 1e-07

PRECISION = lax.Precision.HIGH


def dot(x, y):
    return jnp.dot(x, y, precision=PRECISION, preferred_element_type=jnp.float32)


def gram_of(rows):
    return lax.dot_general(
        rows,
        rows,
        (((0,), (0,)), ((), ())),
        precision=PRECISION,
        preferred_element_type=jnp.float32,
    )


def own_rows(grad, member, tensor_count):
    row_piece = grad.shape[1] // tensor_count
    return lax.dynamic_slice_in_dim(grad, member * row_piece, row_piece, 1)


def shards(grad_square, grad_wide, moment_square, moment_wide):
    tensor_count = lax.axis_size("tensor")
    member = lax.axis_index("tensor")
    count_square, count_wide = grad_square.shape[0], grad_wide.shape[0]
    assert count_square == count_wide and 2 * count_square == tensor_count
    flat_square = own_rows(grad_square, member, tensor_count).astype(jnp.float32)
    flat_wide = own_rows(grad_wide, member, tensor_count).astype(jnp.float32)
    new_square = momentum_decay * moment_square.reshape(flat_square.shape) + flat_square
    new_wide = momentum_decay * moment_wide.reshape(flat_wide.shape) + flat_wide
    look_square = flat_square + momentum_decay * new_square
    look_wide = flat_wide + momentum_decay * new_wide

    piece = look_wide.shape[1]
    pad = piece - look_square.shape[1]
    zeros = jnp.zeros((count_square, pad, look_wide.shape[2]), jnp.float32)
    send = jnp.concatenate([look_wide, look_square, zeros], axis=1).reshape(
        tensor_count, piece, look_wide.shape[2]
    )
    held = lax.all_to_all(send, "tensor", split_axis=0, concat_axis=0, tiled=True)
    rows = held.reshape(tensor_count * piece, held.shape[2])

    gram = lax.psum(gram_of(rows), "shard")
    columns = gram.shape[0]
    eye = jnp.eye(columns, dtype=jnp.float32)
    total = jnp.sum(gram * eye)
    denom = jnp.sqrt(total) + epsilon
    current = rows / denom
    gram = lax.optimization_barrier(gram / (denom * denom))
    for iteration in range(ITERS - 1):
        square_gram = dot(gram, gram)
        mixer = coef_b * gram + coef_c * square_gram
        current = coef_a * current + dot(current, mixer)
        full = mixer + coef_a * eye
        gram = dot(full, dot(gram, full))
    is_square = member % 2 == 1
    scale = jnp.where(
        is_square, jnp.float32(math.sqrt(D)), jnp.float32(math.sqrt(FF))
    )

    def finish(block):
        side = dot(block, gram)
        return scale * (coef_a * block + (coef_b * side + coef_c * dot(side, gram)))

    square_piece = piece - pad
    split = (current.shape[0] + (piece - pad) * tensor_count) // 2
    head, tail = finish(current[:split]), finish(current[split:])
    update = jnp.concatenate([head, tail], axis=0)
    square_rows = update.reshape(tensor_count, piece, -1)[:, :square_piece]
    square_rows = square_rows.reshape(tensor_count * square_piece, -1)
    wide_rows = update.shape[0]
    chunk = (square_rows.shape[0] + wide_rows) // 2
    assert 2 * chunk == square_rows.shape[0] + wide_rows and chunk == split
    to_odd = [(2 * j, 2 * j + 1) for j in range(count_square)]
    handed = lax.ppermute(tail, "tensor", to_odd)
    mine = jnp.where(
        is_square, jnp.concatenate([handed, square_rows], axis=0), head
    )
    gathered = lax.all_gather(mine, "tensor", axis=0, tiled=True)
    gathered = gathered.reshape(count_square, 2 * chunk, update.shape[1])
    update_wide = gathered[:, :wide_rows]
    update_square = gathered[:, wide_rows:]
    return (
        update_square,
        update_wide,
        new_square.reshape(moment_square.shape),
        new_wide.reshape(moment_wide.shape),
    )


def solution(mesh):
    return jax.shard_map(
        shards,
        mesh=mesh,
        in_specs=(
            P(None, "shard", None),
            P(None, "shard", None),
            P(None, ("shard", "tensor")),
            P(None, ("shard", "tensor")),
        ),
        out_specs=(
            P(None, "shard", None),
            P(None, "shard", None),
            P(None, ("shard", "tensor")),
            P(None, ("shard", "tensor")),
        ),
        check_vma=False,
    )
```

```python
import math

import jax
import jax.numpy as jnp
from jax import lax
from jax.sharding import PartitionSpec as P

D = 768
FF = 2048
ITERS = 3


coef_a = 3.4445
coef_b = -4.775
coef_c = 2.0315
momentum_decay = 0.95
epsilon = 1e-07

PRECISION = lax.Precision.HIGH


def dot(x, y):
    return jnp.dot(x, y, precision=PRECISION, preferred_element_type=jnp.float32)


def gram_of(rows):
    return lax.dot_general(
        rows,
        rows,
        (((0,), (0,)), ((), ())),
        precision=PRECISION,
        preferred_element_type=jnp.float32,
    )


def own_rows(grad, member, tensor_count):
    row_piece = grad.shape[1] // tensor_count
    return lax.dynamic_slice_in_dim(grad, member * row_piece, row_piece, 1)


def shards(grad_square, grad_wide, moment_square, moment_wide):
    tensor_count = lax.axis_size("tensor")
    member = lax.axis_index("tensor")
    count_square, count_wide = grad_square.shape[0], grad_wide.shape[0]
    assert count_square == count_wide and 2 * count_square == tensor_count
    flat_square = own_rows(grad_square, member, tensor_count).astype(jnp.float32)
    flat_wide = own_rows(grad_wide, member, tensor_count).astype(jnp.float32)
    new_square = momentum_decay * moment_square.reshape(flat_square.shape) + flat_square
    new_wide = momentum_decay * moment_wide.reshape(flat_wide.shape) + flat_wide
    look_square = flat_square + momentum_decay * new_square
    look_wide = flat_wide + momentum_decay * new_wide

    piece = look_wide.shape[1]
    pad = piece - look_square.shape[1]
    zeros = jnp.zeros((count_square, pad, look_wide.shape[2]), jnp.float32)
    send = jnp.concatenate([look_wide, look_square, zeros], axis=1).reshape(
        tensor_count, piece, look_wide.shape[2]
    )
    held = lax.all_to_all(send, "tensor", split_axis=0, concat_axis=0, tiled=True)
    rows = held.reshape(tensor_count * piece, held.shape[2])

    part = gram_of(rows)
    columns = part.shape[0]
    slab = jnp.zeros((8, columns), jnp.float32).at[0].set(jnp.sum(rows * rows, axis=0))
    packed = lax.psum(jnp.concatenate([part, slab], axis=0), "shard")
    gram = packed[:columns]
    eye = jnp.eye(columns, dtype=jnp.float32)
    total = jnp.sum(packed[columns])
    denom = jnp.sqrt(total) + epsilon
    current = rows / denom
    gram = lax.optimization_barrier(gram / (denom * denom))
    for iteration in range(ITERS - 1):
        square_gram = dot(gram, gram)
        mixer = coef_b * gram + coef_c * square_gram
        current = coef_a * current + dot(current, mixer)
        full = mixer + coef_a * eye
        gram = dot(full, dot(gram, full))
    is_square = member % 2 == 1
    scale = jnp.where(
        is_square, jnp.float32(math.sqrt(D)), jnp.float32(math.sqrt(FF))
    )

    def finish(block):
        side = dot(block, gram)
        return scale * (coef_a * block + (coef_b * side + coef_c * dot(side, gram)))

    square_piece = piece - pad
    split = (current.shape[0] + (piece - pad) * tensor_count) // 2
    head, tail = finish(current[:split]), finish(current[split:])
    update = jnp.concatenate([head, tail], axis=0)
    square_rows = update.reshape(tensor_count, piece, -1)[:, :square_piece]
    square_rows = square_rows.reshape(tensor_count * square_piece, -1)
    wide_rows = update.shape[0]
    chunk = (square_rows.shape[0] + wide_rows) // 2
    assert 2 * chunk == square_rows.shape[0] + wide_rows and chunk == split
    to_odd = [(2 * j, 2 * j + 1) for j in range(count_square)]
    handed = lax.ppermute(tail, "tensor", to_odd)
    mine = jnp.where(
        is_square, jnp.concatenate([handed, square_rows], axis=0), head
    )
    gathered = lax.all_gather(mine, "tensor", axis=0, tiled=True)
    gathered = gathered.reshape(count_square, 2 * chunk, update.shape[1])
    update_wide = gathered[:, :wide_rows]
    update_square = gathered[:, wide_rows:]
    return (
        update_square,
        update_wide,
        new_square.reshape(moment_square.shape),
        new_wide.reshape(moment_wide.shape),
    )


def solution(mesh):
    return jax.shard_map(
        shards,
        mesh=mesh,
        in_specs=(
            P(None, "shard", None),
            P(None, "shard", None),
            P(None, ("shard", "tensor")),
            P(None, ("shard", "tensor")),
        ),
        out_specs=(
            P(None, "shard", None),
            P(None, "shard", None),
            P(None, ("shard", "tensor")),
            P(None, ("shard", "tensor")),
        ),
        check_vma=False,
    )
```

```python
import math

import jax
import jax.numpy as jnp
from jax import lax
from jax.sharding import PartitionSpec as P

D = 768
FF = 2048
ITERS = 3


coef_a = 3.4445
coef_b = -4.775
coef_c = 2.0315
momentum_decay = 0.95
epsilon = 1e-07

PRECISION = lax.Precision.HIGH


def dot(x, y):
    return jnp.dot(x, y, precision=PRECISION, preferred_element_type=jnp.float32)


def gram_of(rows):
    return lax.dot_general(
        rows,
        rows,
        (((0,), (0,)), ((), ())),
        precision=PRECISION,
        preferred_element_type=jnp.float32,
    )


def own_rows(grad, member, tensor_count):
    row_piece = grad.shape[1] // tensor_count
    return lax.dynamic_slice_in_dim(grad, member * row_piece, row_piece, 1)


def shards(grad_square, grad_wide, moment_square, moment_wide):
    tensor_count = lax.axis_size("tensor")
    member = lax.axis_index("tensor")
    count_square, count_wide = grad_square.shape[0], grad_wide.shape[0]
    assert count_square == count_wide and 2 * count_square == tensor_count
    flat_square = own_rows(grad_square, member, tensor_count).astype(jnp.float32)
    flat_wide = own_rows(grad_wide, member, tensor_count).astype(jnp.float32)
    new_square = momentum_decay * moment_square.reshape(flat_square.shape) + flat_square
    new_wide = momentum_decay * moment_wide.reshape(flat_wide.shape) + flat_wide
    look_square = flat_square + momentum_decay * new_square
    look_wide = flat_wide + momentum_decay * new_wide

    piece = look_wide.shape[1]
    pad = piece - look_square.shape[1]
    zeros = jnp.zeros((count_square, pad, look_wide.shape[2]), jnp.float32)
    send = jnp.concatenate([look_wide, look_square, zeros], axis=1).reshape(
        tensor_count, piece, look_wide.shape[2]
    )
    held = lax.all_to_all(send, "tensor", split_axis=0, concat_axis=0, tiled=True)
    rows = held.reshape(tensor_count * piece, held.shape[2])

    gram = lax.psum(gram_of(rows), "shard")
    columns = gram.shape[0]
    eye = jnp.eye(columns, dtype=jnp.float32)
    total = jnp.sum(lax.optimization_barrier(jnp.sum(gram * eye, axis=0)))
    denom = jnp.sqrt(total) + epsilon
    current = rows / denom
    gram = lax.optimization_barrier(gram / (denom * denom))
    for iteration in range(ITERS - 1):
        square_gram = dot(gram, gram)
        mixer = coef_b * gram + coef_c * square_gram
        current = coef_a * current + dot(current, mixer)
        full = mixer + coef_a * eye
        gram = dot(full, dot(gram, full))
    is_square = member % 2 == 1
    scale = jnp.where(
        is_square, jnp.float32(math.sqrt(D)), jnp.float32(math.sqrt(FF))
    )

    def finish(block):
        side = dot(block, gram)
        return scale * (coef_a * block + (coef_b * side + coef_c * dot(side, gram)))

    square_piece = piece - pad
    split = (current.shape[0] + (piece - pad) * tensor_count) // 2
    head, tail = finish(current[:split]), finish(current[split:])
    update = jnp.concatenate([head, tail], axis=0)
    square_rows = update.reshape(tensor_count, piece, -1)[:, :square_piece]
    square_rows = square_rows.reshape(tensor_count * square_piece, -1)
    wide_rows = update.shape[0]
    chunk = (square_rows.shape[0] + wide_rows) // 2
    assert 2 * chunk == square_rows.shape[0] + wide_rows and chunk == split
    to_odd = [(2 * j, 2 * j + 1) for j in range(count_square)]
    handed = lax.ppermute(tail, "tensor", to_odd)
    mine = jnp.where(
        is_square, jnp.concatenate([handed, square_rows], axis=0), head
    )
    gathered = lax.all_gather(mine, "tensor", axis=0, tiled=True)
    gathered = gathered.reshape(count_square, 2 * chunk, update.shape[1])
    update_wide = gathered[:, :wide_rows]
    update_square = gathered[:, wide_rows:]
    return (
        update_square,
        update_wide,
        new_square.reshape(moment_square.shape),
        new_wide.reshape(moment_wide.shape),
    )


def solution(mesh):
    return jax.shard_map(
        shards,
        mesh=mesh,
        in_specs=(
            P(None, "shard", None),
            P(None, "shard", None),
            P(None, ("shard", "tensor")),
            P(None, ("shard", "tensor")),
        ),
        out_specs=(
            P(None, "shard", None),
            P(None, "shard", None),
            P(None, ("shard", "tensor")),
            P(None, ("shard", "tensor")),
        ),
        check_vma=False,
    )
```
